256 devices in a mesh: shard: 64 (over y, z, core), cent: 4 (over x).
Axes of the slice: x: 4, y: 4, z: 8, core: 2. Of those that a mesh axis runs over, the one named last changes fastest.
Arguments:
- queries: bfloat16 [1024, 32, 128], P('shard'), may hold values from -6 to 6
- centroids: bfloat16 [196608, 128], P(('shard', 'cent')), may hold values from -0.5 to 0.5
- passages: bfloat16 [16384, 128, 128], P('shard', 'cent'), may hold values from -0.5 to 0.5
- lengths: int32 [16384], P('shard'), may hold values from 16 to 128, as said below
- passage_row: int32 [16384], replicated, may hold values from 0 to 16383, as said below
- candidates: int32 [1024, 16], P('shard'), may hold values from 0 to 16383, as said below
Outputs:
- token_best: float32 [1024, 32], P('shard')
- scores: float32 [1024, 16], P('shard')
The draws below stay inside these ranges and needn't reach their ends.
Inputs may be any that keep to these rules, and one draw needn't show every extreme that they name: A permutation: passage g is stored at row passage_row[g]. The rows j < lengths[r] of stored passage r are real, the rest padding; the first stored passage of every index of shard has all 128. Among the 256 pairs of the queries of one index of shard, at most 12 have candidates stored at one owner (owner = passage_row[id] // 256); one owner takes exactly 12 pairs from every index of shard.
All inputs are finite; a program needn't handle non-finite values.
Results may differ from the reference program's by a relative error of at most 0.0003.
Values may be sent and summed in bfloat16 or wider, within the bound.
No kernel may reach another device: no remote copies, remote signals or barrier semaphores. Data moves between devices by JAX's collectives and lax.ppermute only.
A program may use at most 128 MiB of HBM per device.

```python
import jax
import jax.numpy as jnp
from jax import lax

D = 128
QT = 32
PT = 128
CAND = 16
Q_DEV = 16
P_DEV = 256
CENT_DEV = 768
NQ = 1024
NP = 16384
NCENT = 196608
CAP = 12


def layout_tables(key):
    row_order = jax.random.permutation(jax.random.fold_in(key, 11), NP).astype(jnp.int32)
    shard_total = NQ // Q_DEV
    pair_total = Q_DEV * CAND
    hot_owner = jax.random.randint(jax.random.fold_in(key, 12), (), 0, shard_total, dtype=jnp.int32)
    spread_keys = jax.random.split(jax.random.fold_in(key, 13), shard_total)

    def spread_one(sub_key):
        return jax.random.permutation(sub_key, (shard_total - 1) * CAP)[:pair_total - CAP].astype(jnp.int32)
    spread = jax.vmap(spread_one)(spread_keys) // CAP
    others = spread + (spread >= hot_owner).astype(jnp.int32)
    owners = jnp.concatenate([jnp.full((shard_total, CAP), hot_owner, jnp.int32), others], axis=1)
    mixing_keys = jax.random.split(jax.random.fold_in(key, 14), shard_total)

    def mixing_one(sub_key):
        return jax.random.permutation(sub_key, pair_total).astype(jnp.int32)
    mixing = jax.vmap(mixing_one)(mixing_keys)
    owners = jnp.take_along_axis(owners, mixing, axis=1)
    slot_ids = jax.random.randint(jax.random.fold_in(key, 15), (shard_total, pair_total), 0, P_DEV, dtype=jnp.int32)
    store_rows = owners * P_DEV + slot_ids
    inverse = jnp.argsort(row_order).astype(jnp.int32)
    chosen_ids = jnp.take(inverse, store_rows.reshape(-1), axis=0).reshape(NQ, CAND)
    return (row_order, chosen_ids)


def draw_passage_row(key, part):
    return layout_tables(key)[0]


def draw_candidates(key, part):
    return layout_tables(key)[1]


def draw_lengths(key, part):
    drawn = jax.random.randint(key, (NP,), PT // 8, PT + 1, dtype=jnp.int32)
    return drawn.at[::P_DEV].set(PT).astype(jnp.int32)


def block_scale(stream_key, shape, cuts, smallest, top_value):
    def one(dim, shards_of):
        draws = jax.random.uniform(jax.random.fold_in(jax.random.fold_in(stream_key, 6), dim), (shards_of,), jnp.float32, smallest / len(cuts), top_value / len(cuts))
        return jnp.repeat(jnp.exp(draws), shape[dim] // shards_of).reshape((-1,) + (1,) * (len(shape) - dim - 1))

    loudness = one(*cuts[0])
    for cut in cuts[1:]:
        loudness = loudness * one(*cut)
    return loudness


def gaussian(stream_key, dims, scale, reach, cuts=(), held_as=jnp.bfloat16):
    gain = block_scale(stream_key, dims, cuts, -0.22, 0.18) if cuts else 1.0
    result = jax.random.normal(stream_key, dims, jnp.float32) * scale * gain
    return jnp.minimum(jnp.maximum(result, -reach), reach).astype(held_as)


def setup_inputs(seed: int = 0) -> dict:
    arg_keys = jax.random.split(jax.random.key(seed), 7)
    queries = gaussian(arg_keys[0], (NQ, QT, D), 1.0, 6.0, ((0, 64),))
    centroids = gaussian(arg_keys[1], (NCENT, D), D ** -0.5, 0.5, ((0, 256),))
    passages = gaussian(arg_keys[2], (NP, PT, D), D ** -0.5, 0.5, ((0, 64), (1, 4)))
    lengths = draw_lengths(jax.random.fold_in(arg_keys[6], 71), 0)
    passage_row = draw_passage_row(jax.random.fold_in(arg_keys[6], 71), 0)
    candidates = draw_candidates(jax.random.fold_in(arg_keys[6], 71), 0)
    return dict(queries=queries, centroids=centroids, passages=passages, lengths=lengths, passage_row=passage_row, candidates=candidates)


def reference(queries, centroids, passages, lengths, passage_row, candidates):
    feature_width = queries.shape[2]
    flattened = queries.reshape(-1, feature_width)
    centroid_blocks = centroids.reshape(-1, CENT_DEV, feature_width)

    def best_step(running, centroid_block):
        scored = jnp.dot(flattened, centroid_block.T, preferred_element_type=jnp.float32)
        return jnp.maximum(running, jnp.max(scored, axis=1)), None

    start_best = jnp.full((flattened.shape[0],), -jnp.inf, jnp.float32)
    running, unused = lax.scan(best_step, start_best, centroid_blocks)
    token_best = running.reshape(NQ, QT)

    pair_rows = jnp.take(passage_row, candidates, axis=0)
    token_index = jnp.arange(PT, dtype=jnp.int32)

    def one_query(query_item):
        query_rows, rows_here = query_item
        chosen = jnp.take(passages, rows_here, axis=0)
        scored = jnp.einsum("td,kpd->ktp", query_rows.astype(jnp.float32), chosen.astype(jnp.float32), precision=lax.Precision.HIGHEST)
        valid_tokens = token_index[None, :] < jnp.take(lengths, rows_here, axis=0)[:, None]
        scored = jnp.where(valid_tokens[:, None, :], scored, -jnp.inf)
        return jnp.sum(jnp.max(scored, axis=2), axis=1) / QT

    scores = lax.map(one_query, (queries, pair_rows))
    return token_best, scores
```

```python
import jax
import jax.numpy as jnp
from jax import lax
from jax.sharding import PartitionSpec as P

masked_score = -1e30


def per_device(queries, centroids, passages, lengths, passage_row, candidates):
    query_count = queries.shape[0]
    query_tokens = queries.shape[1]
    feature_width = queries.shape[2]
    per_query = candidates.shape[1]
    passage_count = passages.shape[0]
    token_rows = passages.shape[1]
    shard_total = lax.axis_size("shard")
    capacity = max(2, 3 * query_count * per_query // shard_total)
    pairs_here = query_count * per_query
    my_shard = lax.axis_index("shard")

    query_block = lax.all_gather(queries, "shard", axis=0, tiled=True)
    cand_block = lax.all_gather(candidates, "shard", axis=0, tiled=True)

    flattened = query_block.reshape(-1, feature_width)
    scored = jnp.einsum("rd,cd->rc", flattened, centroids, preferred_element_type=jnp.float32)
    local_best = jnp.max(scored, axis=1).reshape(shard_total, query_count, query_tokens)
    gathered_best = lax.all_to_all(local_best, "shard", split_axis=0, concat_axis=0, tiled=True)
    shard_best = jnp.max(gathered_best, axis=0)

    all_rows = jnp.take(passage_row, cand_block.reshape(-1), axis=0)
    is_mine = (all_rows // passage_count == my_shard).reshape(shard_total, pairs_here)
    mine_int = is_mine.astype(jnp.int32)
    rank = jnp.cumsum(mine_int, axis=1) - mine_int
    source_ids = jnp.arange(shard_total, dtype=jnp.int32)[:, None]
    places = jnp.where(is_mine, source_ids * capacity + rank, shard_total * capacity).reshape(-1)
    pair_query = jnp.arange(shard_total * pairs_here, dtype=jnp.int32) // per_query
    slot_table = (
        jnp.zeros((shard_total * capacity,), jnp.int32)
        .at[places]
        .set(all_rows % passage_count, mode="drop")
    )
    query_table = (
        jnp.zeros((shard_total * capacity,), jnp.int32).at[places].set(pair_query, mode="drop")
    )
    asked = jnp.take(query_block, query_table, axis=0)
    chosen = jnp.take(passages, slot_table, axis=0)
    pair_scored = jnp.einsum("ntd,npd->ntp", asked, chosen, preferred_element_type=jnp.float32)
    token_index = lax.axis_index("cent") * token_rows + jnp.arange(token_rows, dtype=jnp.int32)
    valid_tokens = token_index[None, :] < jnp.take(lengths, slot_table, axis=0)[:, None]
    pair_scored = jnp.where(valid_tokens[:, None, :], pair_scored, masked_score)
    partial_value = jnp.max(pair_scored, axis=2)

    merged = lax.pmax(
        jnp.concatenate([shard_best, partial_value], axis=0), "cent"
    )
    token_best = merged[:query_count]
    complete = merged[query_count:]
    pair_scores = (jnp.sum(complete, axis=1) / query_tokens).reshape(shard_total, capacity)
    returned = lax.all_to_all(pair_scores, "shard", split_axis=0, concat_axis=0, tiled=True)

    pair_rows = jnp.take(passage_row, candidates.reshape(-1), axis=0)
    owners = pair_rows // passage_count
    onehot = (owners[:, None] == jnp.arange(shard_total, dtype=jnp.int32)[None, :]).astype(
        jnp.int32
    )
    ranking = jnp.sum((jnp.cumsum(onehot, axis=0) - onehot) * onehot, axis=1)
    my_places = owners * capacity + ranking
    scores = jnp.take(returned.reshape(-1), my_places, axis=0).reshape(query_count, per_query)
    return (token_best, scores)


def solution(mesh):
    in_specs = (
        P("shard", None, None),
        P(("shard", "cent"), None),
        P("shard", "cent", None),
        P("shard"),
        P(),
        P("shard", None),
    )
    out_specs = (P("shard", None), P("shard", None))
    return jax.shard_map(
        per_device, mesh=mesh, in_specs=in_specs, out_specs=out_specs, check_vma=False
    )
```

```python
import jax
import jax.numpy as jnp
from jax import lax
from jax.sharding import PartitionSpec as P

masked_score = -1e30


def per_device(queries, centroids, passages, lengths, passage_row, candidates):
    query_count = queries.shape[0]
    query_tokens = queries.shape[1]
    feature_width = queries.shape[2]
    per_query = candidates.shape[1]
    passage_count = passages.shape[0]
    token_rows = passages.shape[1]
    shard_total = lax.axis_size("shard")
    capacity = max(2, 3 * query_count * per_query // shard_total)
    pairs_here = query_count * per_query
    my_shard = lax.axis_index("shard")

    pair_rows = jnp.take(passage_row, candidates.reshape(-1), axis=0)
    owners = pair_rows // passage_count
    onehot = (owners[:, None] == jnp.arange(shard_total, dtype=jnp.int32)[None, :]).astype(
        jnp.int32
    )
    ranking = jnp.sum((jnp.cumsum(onehot, axis=0) - onehot) * onehot, axis=1)
    my_places = owners * capacity + ranking
    pair_local = jnp.arange(pairs_here, dtype=jnp.int32) // per_query
    entries = jnp.stack([pair_rows % passage_count, pair_local], axis=1).astype(jnp.bfloat16)
    table = jnp.full((shard_total * capacity, 2), -1.0, jnp.bfloat16).at[my_places].set(entries)
    row_width = query_tokens * feature_width
    table_rows = -(-(shard_total * capacity * 2) // row_width)
    table = jnp.pad(table.reshape(-1), (0, table_rows * row_width - shard_total * capacity * 2))

    packed = jnp.concatenate(
        [queries.reshape(query_count, row_width), table.reshape(table_rows, row_width)], axis=0
    )
    packed_block = lax.all_gather(packed, "shard", axis=0, tiled=False)
    query_block = packed_block[:, :query_count].reshape(-1, query_tokens, feature_width)
    tables = packed_block[:, query_count:].reshape(shard_total, -1)[:, : shard_total * capacity * 2]
    tables = tables.reshape(shard_total, shard_total, capacity, 2)
    mine = lax.dynamic_index_in_dim(tables, my_shard, axis=1, keepdims=False).astype(jnp.int32)

    flattened = query_block.reshape(-1, feature_width)
    scored = jnp.einsum("rd,cd->rc", flattened, centroids, preferred_element_type=jnp.float32)
    local_best = jnp.max(scored, axis=1).reshape(shard_total, query_count, query_tokens)
    gathered_best = lax.all_to_all(local_best, "shard", split_axis=0, concat_axis=0, tiled=True)
    shard_best = jnp.max(gathered_best, axis=0)

    slot_table = jnp.maximum(mine[..., 0], 0).reshape(-1)
    query_table = (
        jnp.arange(shard_total, dtype=jnp.int32)[:, None] * query_count + jnp.maximum(mine[..., 1], 0)
    ).reshape(-1)
    asked = jnp.take(query_block, query_table, axis=0)
    chosen = jnp.take(passages, slot_table, axis=0)
    pair_scored = jnp.einsum("ntd,npd->ntp", asked, chosen, preferred_element_type=jnp.float32)
    token_index = lax.axis_index("cent") * token_rows + jnp.arange(token_rows, dtype=jnp.int32)
    valid_tokens = token_index[None, :] < jnp.take(lengths, slot_table, axis=0)[:, None]
    pair_scored = jnp.where(valid_tokens[:, None, :], pair_scored, masked_score)
    partial_value = jnp.max(pair_scored, axis=2)

    merged = jnp.concatenate([shard_best, partial_value], axis=0)
    cent_total = lax.axis_size("cent")
    step = 1
    while step < cent_total:
        partner = [(i, i ^ step) for i in range(cent_total)]
        merged = jnp.maximum(merged, lax.ppermute(merged, "cent", partner))
        step *= 2
    token_best = merged[:query_count]
    complete = merged[query_count:]
    pair_scores = (jnp.sum(complete, axis=1) / query_tokens).reshape(shard_total, capacity)
    returned = lax.all_to_all(pair_scores, "shard", split_axis=0, concat_axis=0, tiled=True)

    scores = jnp.take(returned.reshape(-1), my_places, axis=0).reshape(query_count, per_query)
    return (token_best, scores)


def solution(mesh):
    in_specs = (
        P("shard", None, None),
        P(("shard", "cent"), None),
        P("shard", "cent", None),
        P("shard"),
        P(),
        P("shard", None),
    )
    out_specs = (P("shard", None), P("shard", None))
    return jax.shard_map(
        per_device, mesh=mesh, in_specs=in_specs, out_specs=out_specs, check_vma=False
    )
```

```python
import jax
import jax.numpy as jnp
from jax import lax
from jax.sharding import Mesh, PartitionSpec as P

masked_score = -1e30


def per_device(queries, centroids, passages, lengths, passage_row, candidates):
    query_count = queries.shape[0]
    query_tokens = queries.shape[1]
    feature_width = queries.shape[2]
    per_query = candidates.shape[1]
    passage_count = passages.shape[0]
    token_rows = passages.shape[1]
    shard_total = lax.axis_size(("chip", "core"))
    capacity = max(2, 3 * query_count * per_query // shard_total)
    pairs_here = query_count * per_query
    my_shard = lax.axis_index(("chip", "core"))

    pair_rows = jnp.take(passage_row, candidates.reshape(-1), axis=0)
    owners = pair_rows // passage_count
    onehot = (owners[:, None] == jnp.arange(shard_total, dtype=jnp.int32)[None, :]).astype(
        jnp.int32
    )
    ranking = jnp.sum((jnp.cumsum(onehot, axis=0) - onehot) * onehot, axis=1)
    my_places = owners * capacity + ranking
    pair_local = jnp.arange(pairs_here, dtype=jnp.int32) // per_query
    entries = jnp.stack([pair_rows % passage_count, pair_local], axis=1).astype(jnp.bfloat16)
    table = jnp.full((shard_total * capacity, 2), -1.0, jnp.bfloat16).at[my_places].set(entries)
    table = table.reshape(-1)

    tables = lax.all_gather(table, ("chip", "core"), axis=0, tiled=False)
    tables = tables[:, : shard_total * capacity * 2].reshape(shard_total, shard_total, capacity, 2)
    mine = lax.dynamic_index_in_dim(tables, my_shard, axis=1, keepdims=False).astype(jnp.int32)
    core_total = lax.axis_size("core")
    my_core = lax.axis_index("core")
    same_core = lax.all_gather(queries, "chip", axis=0, tiled=False)
    other_core = lax.ppermute(same_core, "core", [(i, (i + 1) % core_total) for i in range(core_total)])
    first, second = (
        jnp.where(my_core == 0, same_core, other_core),
        jnp.where(my_core == 0, other_core, same_core),
    )
    query_block = jnp.stack([first, second], axis=1).reshape(-1, query_tokens, feature_width)

    def block_best(block):
        scored = jnp.einsum("rd,cd->rc", block.reshape(-1, feature_width), centroids,
                            preferred_element_type=jnp.float32)
        return jnp.max(scored, axis=1).reshape(-1, query_count, query_tokens)

    best_same = block_best(same_core)
    best_other = block_best(other_core)
    local_best = jnp.stack(
        [jnp.where(my_core == 0, best_same, best_other), jnp.where(my_core == 0, best_other, best_same)],
        axis=1,
    ).reshape(shard_total, query_count, query_tokens)
    gathered_best = lax.all_to_all(local_best, ("chip", "core"), split_axis=0, concat_axis=0, tiled=True)
    shard_best = jnp.max(gathered_best, axis=0)

    slot_table = jnp.maximum(mine[..., 0], 0).reshape(-1)
    query_table = (
        jnp.arange(shard_total, dtype=jnp.int32)[:, None] * query_count + jnp.maximum(mine[..., 1], 0)
    ).reshape(-1)
    asked = jnp.take(query_block, query_table, axis=0)
    chosen = jnp.take(passages, slot_table, axis=0)
    pair_scored = jnp.einsum("ntd,npd->ntp", asked, chosen, preferred_element_type=jnp.float32)
    token_index = lax.axis_index("cent") * token_rows + jnp.arange(token_rows, dtype=jnp.int32)
    valid_tokens = token_index[None, :] < jnp.take(lengths, slot_table, axis=0)[:, None]
    pair_scored = jnp.where(valid_tokens[:, None, :], pair_scored, masked_score)
    partial_value = jnp.max(pair_scored, axis=2)

    merged = jnp.concatenate([shard_best, partial_value], axis=0)
    cent_total = lax.axis_size("cent")
    step = 1
    while step < cent_total:
        partner = [(i, i ^ step) for i in range(cent_total)]
        merged = jnp.maximum(merged, lax.ppermute(merged, "cent", partner))
        step *= 2
    token_best = merged[:query_count]
    complete = merged[query_count:]
    pair_scores = (jnp.sum(complete, axis=1) / query_tokens).reshape(shard_total, capacity)
    returned = lax.all_to_all(pair_scores, ("chip", "core"), split_axis=0, concat_axis=0, tiled=True)

    scores = jnp.take(returned.reshape(-1), my_places, axis=0).reshape(query_count, per_query)
    return (token_best, scores)


def solution(mesh):
    shard_size, cent_size = mesh.devices.shape
    split_mesh = Mesh(mesh.devices.reshape(shard_size // 2, 2, cent_size), ("chip", "core", "cent"))
    shard = ("chip", "core")
    in_specs = (
        P(shard, None, None),
        P((*shard, "cent"), None),
        P(shard, "cent", None),
        P(shard),
        P(),
        P(shard, None),
    )
    out_specs = (P(shard, None), P(shard, None))
    return jax.shard_map(
        per_device, mesh=split_mesh, in_specs=in_specs, out_specs=out_specs, check_vma=False
    )
```

```python
import jax
import jax.numpy as jnp
from jax import lax
from jax.sharding import PartitionSpec as P

masked_score = -1e30


def per_device(queries, centroids, passages, lengths, passage_row, candidates):
    query_count = queries.shape[0]
    query_tokens = queries.shape[1]
    feature_width = queries.shape[2]
    per_query = candidates.shape[1]
    passage_count = passages.shape[0]
    token_rows = passages.shape[1]
    shard_total = lax.axis_size("shard")
    capacity = max(2, 3 * query_count * per_query // shard_total)
    pairs_here = query_count * per_query
    my_shard = lax.axis_index("shard")

    pair_rows = jnp.take(passage_row, candidates.reshape(-1), axis=0)
    owners = pair_rows // passage_count
    onehot = (owners[:, None] == jnp.arange(shard_total, dtype=jnp.int32)[None, :]).astype(
        jnp.int32
    )
    ranking = jnp.sum((jnp.cumsum(onehot, axis=0) - onehot) * onehot, axis=1)
    my_places = owners * capacity + ranking
    pair_local = jnp.arange(pairs_here, dtype=jnp.int32) // per_query
    entries = jnp.stack([pair_rows % passage_count, my_shard * query_count + pair_local], axis=1)
    table = (
        jnp.full((shard_total * capacity, 2), -1, jnp.int32)
        .at[my_places]
        .set(entries)
        .reshape(shard_total, capacity * 2)
    )

    query_block = lax.all_gather(queries, "shard", axis=0, tiled=True)
    mine = lax.all_to_all(table, "shard", split_axis=0, concat_axis=0, tiled=True).reshape(
        shard_total, capacity, 2
    )

    flattened = query_block.reshape(-1, feature_width)
    scored = jnp.einsum("rd,cd->rc", flattened, centroids, preferred_element_type=jnp.float32)
    local_best = jnp.max(scored, axis=1).reshape(shard_total, query_count, query_tokens)
    gathered_best = lax.all_to_all(local_best, "shard", split_axis=0, concat_axis=0, tiled=True)
    shard_best = jnp.max(gathered_best, axis=0)

    slot_table = jnp.maximum(mine[..., 0], 0).reshape(-1)
    query_table = jnp.maximum(mine[..., 1], 0).reshape(-1)
    asked = jnp.take(query_block, query_table, axis=0)
    chosen = jnp.take(passages, slot_table, axis=0)
    pair_scored = jnp.einsum("ntd,npd->ntp", asked, chosen, preferred_element_type=jnp.float32)
    token_index = lax.axis_index("cent") * token_rows + jnp.arange(token_rows, dtype=jnp.int32)
    valid_tokens = token_index[None, :] < jnp.take(lengths, slot_table, axis=0)[:, None]
    pair_scored = jnp.where(valid_tokens[:, None, :], pair_scored, masked_score)
    partial_value = jnp.max(pair_scored, axis=2)

    merged = jnp.concatenate([shard_best, partial_value], axis=0)
    cent_total = lax.axis_size("cent")
    step = 1
    while step < cent_total:
        partner = [(i, i ^ step) for i in range(cent_total)]
        merged = jnp.maximum(merged, lax.ppermute(merged, "cent", partner))
        step *= 2
    token_best = merged[:query_count]
    complete = merged[query_count:]
    pair_scores = (jnp.sum(complete, axis=1) / query_tokens).reshape(shard_total, capacity)
    returned = lax.all_to_all(pair_scores, "shard", split_axis=0, concat_axis=0, tiled=True)

    scores = jnp.take(returned.reshape(-1), my_places, axis=0).reshape(query_count, per_query)
    return (token_best, scores)


def solution(mesh):
    in_specs = (
        P("shard", None, None),
        P(("shard", "cent"), None),
        P("shard", "cent", None),
        P("shard"),
        P(),
        P("shard", None),
    )
    out_specs = (P("shard", None), P("shard", None))
    return jax.shard_map(
        per_device, mesh=mesh, in_specs=in_specs, out_specs=out_specs, check_vma=False
    )
```

```python
import jax
import jax.numpy as jnp
from jax import lax
from jax.sharding import Mesh, PartitionSpec as P

masked_score = -1e30


shard = ("y", "rest")


def per_device(queries, centroids, passages, lengths, passage_row, candidates):
    query_count = queries.shape[0]
    query_tokens = queries.shape[1]
    feature_width = queries.shape[2]
    per_query = candidates.shape[1]
    passage_count = passages.shape[0]
    token_rows = passages.shape[1]
    shard_total = lax.axis_size(shard)
    capacity = max(2, 3 * query_count * per_query // shard_total)
    pairs_here = query_count * per_query
    my_shard = lax.axis_index(shard)

    pair_rows = jnp.take(passage_row, candidates.reshape(-1), axis=0)
    owners = pair_rows // passage_count
    onehot = (owners[:, None] == jnp.arange(shard_total, dtype=jnp.int32)[None, :]).astype(
        jnp.int32
    )
    ranking = jnp.sum((jnp.cumsum(onehot, axis=0) - onehot) * onehot, axis=1)
    my_places = owners * capacity + ranking
    pair_local = jnp.arange(pairs_here, dtype=jnp.int32) // per_query
    entries = jnp.stack([pair_rows % passage_count, my_shard * query_count + pair_local], axis=1)
    table = (
        jnp.full((shard_total * capacity, 2), -1, jnp.int32)
        .at[my_places]
        .set(entries)
        .reshape(shard_total, capacity * 2)
    )

    query_block = lax.all_gather(
        lax.all_gather(queries, "y", axis=0, tiled=True), "rest", axis=0, tiled=True
    )
    y_total = lax.axis_size("y")
    rest_total = lax.axis_size("rest")
    mine = lax.all_to_all(table, shard, split_axis=0, concat_axis=0, tiled=True).reshape(
        shard_total, capacity, 2
    )

    flattened = query_block.reshape(-1, feature_width)
    scored = jnp.einsum("rd,cd->rc", flattened, centroids, preferred_element_type=jnp.float32)
    local_best = (
        jnp.max(scored, axis=1)
        .reshape(rest_total, y_total, query_count, query_tokens)
        .transpose(1, 0, 2, 3)
        .reshape(shard_total, query_count, query_tokens)
    )
    gathered_best = lax.all_to_all(local_best, shard, split_axis=0, concat_axis=0, tiled=True)
    shard_best = jnp.max(gathered_best, axis=0)

    slot_table = jnp.maximum(mine[..., 0], 0).reshape(-1)
    global_query = jnp.maximum(mine[..., 1], 0).reshape(-1)
    source_shard = global_query // query_count
    query_table = (
        (source_shard % rest_total) * y_total + source_shard // rest_total
    ) * query_count + global_query % query_count
    asked = jnp.take(query_block, query_table, axis=0)
    chosen = jnp.take(passages, slot_table, axis=0)
    pair_scored = jnp.einsum("ntd,npd->ntp", asked, chosen, preferred_element_type=jnp.float32)
    token_index = lax.axis_index("cent") * token_rows + jnp.arange(token_rows, dtype=jnp.int32)
    valid_tokens = token_index[None, :] < jnp.take(lengths, slot_table, axis=0)[:, None]
    pair_scored = jnp.where(valid_tokens[:, None, :], pair_scored, masked_score)
    partial_value = jnp.max(pair_scored, axis=2)

    merged = jnp.concatenate([shard_best, partial_value], axis=0)
    cent_total = lax.axis_size("cent")
    step = 1
    while step < cent_total:
        partner = [(i, i ^ step) for i in range(cent_total)]
        merged = jnp.maximum(merged, lax.ppermute(merged, "cent", partner))
        step *= 2
    token_best = merged[:query_count]
    complete = merged[query_count:]
    pair_scores = (jnp.sum(complete, axis=1) / query_tokens).reshape(shard_total, capacity)
    returned = lax.all_to_all(pair_scores, shard, split_axis=0, concat_axis=0, tiled=True)

    scores = jnp.take(returned.reshape(-1), my_places, axis=0).reshape(query_count, per_query)
    return (token_best, scores)


def solution(mesh):
    shard_size, cent_size = mesh.devices.shape
    y_size = len({d.coords[1] for d in mesh.devices.flat})
    split_mesh = Mesh(
        mesh.devices.reshape(y_size, shard_size // y_size, cent_size), ("y", "rest", "cent")
    )
    in_specs = (
        P(shard, None, None),
        P((*shard, "cent"), None),
        P(shard, "cent", None),
        P(shard),
        P(),
        P(shard, None),
    )
    out_specs = (P(shard, None), P(shard, None))
    return jax.shard_map(
        per_device, mesh=split_mesh, in_specs=in_specs, out_specs=out_specs, check_vma=False
    )
```

```python
import jax
import jax.numpy as jnp
from jax import lax
from jax.sharding import Mesh, PartitionSpec as P

masked_score = -1e30


shard = ("y", "rest")


def per_device(queries, centroids, passages, lengths, passage_row, candidates):
    query_count = queries.shape[0]
    query_tokens = queries.shape[1]
    feature_width = queries.shape[2]
    per_query = candidates.shape[1]
    passage_count = passages.shape[0]
    token_rows = passages.shape[1]
    shard_total = lax.axis_size(shard)
    capacity = max(2, 3 * query_count * per_query // shard_total)
    pairs_here = query_count * per_query
    my_shard = lax.axis_index(shard)

    pair_rows = jnp.take(passage_row, candidates.reshape(-1), axis=0)
    owners = pair_rows // passage_count
    onehot = (owners[:, None] == jnp.arange(shard_total, dtype=jnp.int32)[None, :]).astype(
        jnp.int32
    )
    ranking = jnp.sum((jnp.cumsum(onehot, axis=0) - onehot) * onehot, axis=1)
    my_places = owners * capacity + ranking
    pair_local = jnp.arange(pairs_here, dtype=jnp.int32) // per_query
    entries = jnp.stack([pair_rows % passage_count, my_shard * query_count + pair_local], axis=1)
    table = (
        jnp.full((shard_total * capacity, 2), -1, jnp.int32)
        .at[my_places]
        .set(entries)
        .reshape(shard_total, capacity * 2)
    )

    query_block = lax.all_gather(
        lax.all_gather(queries, "y", axis=0, tiled=True), "rest", axis=0, tiled=True
    )
    y_total = lax.axis_size("y")
    rest_total = lax.axis_size("rest")
    mine = lax.all_to_all(table, shard, split_axis=0, concat_axis=0, tiled=True).reshape(
        shard_total, capacity, 2
    )

    flattened = query_block.reshape(-1, feature_width)
    scored = jnp.einsum("rd,cd->rc", flattened, centroids, preferred_element_type=jnp.float32)
    local_best = (
        jnp.max(scored, axis=1)
        .reshape(rest_total, y_total, query_count, query_tokens)
        .transpose(1, 0, 2, 3)
        .reshape(shard_total, query_count, query_tokens)
    )
    gathered_best = lax.all_to_all(local_best, shard, split_axis=0, concat_axis=0, tiled=True)
    shard_best = jnp.max(gathered_best, axis=0)

    slot_table = jnp.maximum(mine[..., 0], 0).reshape(-1)
    global_query = jnp.maximum(mine[..., 1], 0).reshape(-1)
    source_shard = global_query // query_count
    query_table = (
        (source_shard % rest_total) * y_total + source_shard // rest_total
    ) * query_count + global_query % query_count
    asked = jnp.take(query_block, query_table, axis=0)
    chosen = jnp.take(passages, slot_table, axis=0)
    pair_scored = jnp.einsum("ntd,npd->ntp", asked, chosen, preferred_element_type=jnp.float32)
    token_index = lax.axis_index("cent") * token_rows + jnp.arange(token_rows, dtype=jnp.int32)
    valid_tokens = token_index[None, :] < jnp.take(lengths, slot_table, axis=0)[:, None]
    pair_scored = jnp.where(valid_tokens[:, None, :], pair_scored, masked_score)
    partial_value = jnp.max(pair_scored, axis=2)

    merged = jnp.concatenate([shard_best, partial_value], axis=0)
    cent_total = lax.axis_size("cent")
    arrived = [
        lax.ppermute(merged, "cent", [(i, (i + shift) % cent_total) for i in range(cent_total)])
        for shift in range(1, cent_total)
    ]
    for other in arrived:
        merged = jnp.maximum(merged, other)
    token_best = merged[:query_count]
    complete = merged[query_count:]
    pair_scores = (jnp.sum(complete, axis=1) / query_tokens).reshape(shard_total, capacity)
    returned = lax.all_to_all(pair_scores, shard, split_axis=0, concat_axis=0, tiled=True)

    scores = jnp.take(returned.reshape(-1), my_places, axis=0).reshape(query_count, per_query)
    return (token_best, scores)


def solution(mesh):
    shard_size, cent_size = mesh.devices.shape
    y_size = len({d.coords[1] for d in mesh.devices.flat})
    split_mesh = Mesh(
        mesh.devices.reshape(y_size, shard_size // y_size, cent_size), ("y", "rest", "cent")
    )
    in_specs = (
        P(shard, None, None),
        P((*shard, "cent"), None),
        P(shard, "cent", None),
        P(shard),
        P(),
        P(shard, None),
    )
    out_specs = (P(shard, None), P(shard, None))
    return jax.shard_map(
        per_device, mesh=split_mesh, in_specs=in_specs, out_specs=out_specs, check_vma=False
    )
```

```python
import jax
import jax.numpy as jnp
from jax import lax
from jax.sharding import Mesh, PartitionSpec as P

masked_score = -1e30


shard = ("y", "rest")


def per_device(queries, centroids, passages, lengths, passage_row, candidates):
    query_count = queries.shape[0]
    query_tokens = queries.shape[1]
    feature_width = queries.shape[2]
    per_query = candidates.shape[1]
    passage_count = passages.shape[0]
    token_rows = passages.shape[1]
    shard_total = lax.axis_size(shard)
    capacity = max(2, 3 * query_count * per_query // shard_total)
    pairs_here = query_count * per_query
    my_shard = lax.axis_index(shard)

    pair_rows = jnp.take(passage_row, candidates.reshape(-1), axis=0)
    owners = pair_rows // passage_count
    onehot = (owners[:, None] == jnp.arange(shard_total, dtype=jnp.int32)[None, :]).astype(
        jnp.int32
    )
    ranking = jnp.sum((jnp.cumsum(onehot, axis=0) - onehot) * onehot, axis=1)
    my_places = owners * capacity + ranking
    pair_local = jnp.arange(pairs_here, dtype=jnp.int32) // per_query
    entries = jnp.stack([pair_rows % passage_count, my_shard * query_count + pair_local], axis=1)
    table = (
        jnp.full((shard_total * capacity, 2), -1, jnp.int32)
        .at[my_places]
        .set(entries)
        .reshape(shard_total, capacity * 2)
    )

    mine = lax.all_to_all(table, shard, split_axis=0, concat_axis=0, tiled=True).reshape(
        shard_total, capacity, 2
    )
    slot_table = jnp.maximum(mine[..., 0], 0).reshape(-1)
    global_query = jnp.maximum(mine[..., 1], 0).reshape(-1)
    chosen = jnp.take(passages, slot_table, axis=0)
    token_index = lax.axis_index("cent") * token_rows + jnp.arange(token_rows, dtype=jnp.int32)
    valid_tokens = token_index[None, :] < jnp.take(lengths, slot_table, axis=0)[:, None]

    y_total = lax.axis_size("y")
    rest_total = lax.axis_size("rest")
    part_total = 2 if y_total % 2 == 0 else 1
    y_part = y_total // part_total
    along_y = lax.all_gather(queries, "y", axis=0, tiled=True)
    part_best = []
    part_value = []
    pairs_per_part = shard_total * capacity // part_total
    for part in range(part_total):
        block = lax.all_gather(
            along_y[part * y_part * query_count:(part + 1) * y_part * query_count],
            "rest", axis=0, tiled=True,
        )
        scored = jnp.einsum("rd,cd->rc", block.reshape(-1, feature_width), centroids,
                            preferred_element_type=jnp.float32)
        part_best.append(
            jnp.max(scored, axis=1).reshape(rest_total, y_part, query_count, query_tokens)
        )
        rows = slice(part * pairs_per_part, (part + 1) * pairs_per_part)
        query_here = global_query[rows]
        source_shard = query_here // query_count
        query_table = (
            (source_shard % rest_total) * y_part + source_shard // rest_total - part * y_part
        ) * query_count + query_here % query_count
        asked = jnp.take(block, query_table, axis=0)
        pair_scored = jnp.einsum("ntd,npd->ntp", asked, chosen[rows],
                                 preferred_element_type=jnp.float32)
        pair_scored = jnp.where(valid_tokens[rows][:, None, :], pair_scored, masked_score)
        part_value.append(jnp.max(pair_scored, axis=2))

    local_best = (
        jnp.stack(part_best, axis=0)
        .transpose(0, 2, 1, 3, 4)
        .reshape(shard_total, query_count, query_tokens)
    )
    gathered_best = lax.all_to_all(local_best, shard, split_axis=0, concat_axis=0, tiled=True)
    shard_best = jnp.max(gathered_best, axis=0)
    partial_value = jnp.concatenate(part_value, axis=0)

    merged = jnp.concatenate([shard_best, partial_value], axis=0)
    cent_total = lax.axis_size("cent")
    arrived = [
        lax.ppermute(merged, "cent", [(i, (i + shift) % cent_total) for i in range(cent_total)])
        for shift in range(1, cent_total)
    ]
    for other in arrived:
        merged = jnp.maximum(merged, other)
    token_best = merged[:query_count]
    complete = merged[query_count:]
    pair_scores = (jnp.sum(complete, axis=1) / query_tokens).reshape(shard_total, capacity)
    returned = lax.all_to_all(pair_scores, shard, split_axis=0, concat_axis=0, tiled=True)

    scores = jnp.take(returned.reshape(-1), my_places, axis=0).reshape(query_count, per_query)
    return (token_best, scores)


def solution(mesh):
    shard_size, cent_size = mesh.devices.shape
    y_size = len({d.coords[1] for d in mesh.devices.flat})
    split_mesh = Mesh(
        mesh.devices.reshape(y_size, shard_size // y_size, cent_size), ("y", "rest", "cent")
    )
    in_specs = (
        P(shard, None, None),
        P((*shard, "cent"), None),
        P(shard, "cent", None),
        P(shard),
        P(),
        P(shard, None),
    )
    out_specs = (P(shard, None), P(shard, None))
    return jax.shard_map(
        per_device, mesh=split_mesh, in_specs=in_specs, out_specs=out_specs, check_vma=False
    )
```

```python
import jax
import jax.numpy as jnp
from jax import lax
from jax.sharding import Mesh, PartitionSpec as P

masked_score = -1e30


shard = ("y", "rest")


def per_device(queries, centroids, passages, lengths, passage_row, candidates):
    query_count = queries.shape[0]
    query_tokens = queries.shape[1]
    feature_width = queries.shape[2]
    per_query = candidates.shape[1]
    passage_count = passages.shape[0]
    token_rows = passages.shape[1]
    shard_total = lax.axis_size(shard)
    capacity = max(2, 3 * query_count * per_query // shard_total)
    pairs_here = query_count * per_query
    my_shard = lax.axis_index(shard)

    pair_rows = jnp.take(passage_row, candidates.reshape(-1), axis=0)
    owners = pair_rows // passage_count
    onehot = (owners[:, None] == jnp.arange(shard_total, dtype=jnp.int32)[None, :]).astype(
        jnp.int32
    )
    ranking = jnp.sum((jnp.cumsum(onehot, axis=0) - onehot) * onehot, axis=1)
    my_places = owners * capacity + ranking
    pair_local = jnp.arange(pairs_here, dtype=jnp.int32) // per_query
    entries = jnp.stack([pair_rows % passage_count, my_shard * query_count + pair_local], axis=1)
    table = (
        jnp.full((shard_total * capacity, 2), -1, jnp.int32)
        .at[my_places]
        .set(entries)
        .reshape(shard_total, capacity * 2)
    )

    y_total = lax.axis_size("y")
    rest_total = lax.axis_size("rest")
    my_y = lax.axis_index("y")
    along_y = [queries] + [
        lax.ppermute(queries, "y", [(i, (i + shift) % y_total) for i in range(y_total)])
        for shift in range(1, y_total)
    ]
    query_block = lax.all_gather(
        jnp.concatenate(along_y, axis=0), "rest", axis=0, tiled=True
    )
    mine = lax.all_to_all(table, shard, split_axis=0, concat_axis=0, tiled=True).reshape(
        shard_total, capacity, 2
    )

    flattened = query_block.reshape(-1, feature_width)
    scored = jnp.einsum("rd,cd->rc", flattened, centroids, preferred_element_type=jnp.float32)
    by_shift = jnp.max(scored, axis=1).reshape(rest_total, y_total, query_count, query_tokens)
    shift_of_y = (my_y - jnp.arange(y_total, dtype=jnp.int32)) % y_total
    local_best = (
        jnp.take(by_shift, shift_of_y, axis=1)
        .transpose(1, 0, 2, 3)
        .reshape(shard_total, query_count, query_tokens)
    )
    gathered_best = lax.all_to_all(local_best, shard, split_axis=0, concat_axis=0, tiled=True)
    shard_best = jnp.max(gathered_best, axis=0)

    slot_table = jnp.maximum(mine[..., 0], 0).reshape(-1)
    global_query = jnp.maximum(mine[..., 1], 0).reshape(-1)
    source_shard = global_query // query_count
    query_table = (
        (source_shard % rest_total) * y_total + (my_y - source_shard // rest_total) % y_total
    ) * query_count + global_query % query_count
    asked = jnp.take(query_block, query_table, axis=0)
    chosen = jnp.take(passages, slot_table, axis=0)
    pair_scored = jnp.einsum("ntd,npd->ntp", asked, chosen, preferred_element_type=jnp.float32)
    token_index = lax.axis_index("cent") * token_rows + jnp.arange(token_rows, dtype=jnp.int32)
    valid_tokens = token_index[None, :] < jnp.take(lengths, slot_table, axis=0)[:, None]
    pair_scored = jnp.where(valid_tokens[:, None, :], pair_scored, masked_score)
    partial_value = jnp.max(pair_scored, axis=2)

    merged = jnp.concatenate([shard_best, partial_value], axis=0)
    cent_total = lax.axis_size("cent")
    arrived = [
        lax.ppermute(merged, "cent", [(i, (i + shift) % cent_total) for i in range(cent_total)])
        for shift in range(1, cent_total)
    ]
    for other in arrived:
        merged = jnp.maximum(merged, other)
    token_best = merged[:query_count]
    complete = merged[query_count:]
    pair_scores = (jnp.sum(complete, axis=1) / query_tokens).reshape(shard_total, capacity)
    returned = lax.all_to_all(pair_scores, shard, split_axis=0, concat_axis=0, tiled=True)

    scores = jnp.take(returned.reshape(-1), my_places, axis=0).reshape(query_count, per_query)
    return (token_best, scores)


def solution(mesh):
    shard_size, cent_size = mesh.devices.shape
    y_size = len({d.coords[1] for d in mesh.devices.flat})
    split_mesh = Mesh(
        mesh.devices.reshape(y_size, shard_size // y_size, cent_size), ("y", "rest", "cent")
    )
    in_specs = (
        P(shard, None, None),
        P((*shard, "cent"), None),
        P(shard, "cent", None),
        P(shard),
        P(),
        P(shard, None),
    )
    out_specs = (P(shard, None), P(shard, None))
    return jax.shard_map(
        per_device, mesh=split_mesh, in_specs=in_specs, out_specs=out_specs, check_vma=False
    )
```

```python
import jax
import jax.numpy as jnp
from jax import lax
from jax.sharding import Mesh, PartitionSpec as P

masked_score = -1e30


shard = ("y", "rest")


def per_device(queries, centroids, passages, lengths, passage_row, candidates):
    query_count = queries.shape[0]
    query_tokens = queries.shape[1]
    feature_width = queries.shape[2]
    per_query = candidates.shape[1]
    passage_count = passages.shape[0]
    token_rows = passages.shape[1]
    shard_total = lax.axis_size(shard)
    capacity = max(2, 3 * query_count * per_query // shard_total)
    pairs_here = query_count * per_query
    my_shard = lax.axis_index(shard)

    pair_rows = jnp.take(passage_row, candidates.reshape(-1), axis=0)
    owners = pair_rows // passage_count
    onehot = (owners[:, None] == jnp.arange(shard_total, dtype=jnp.int32)[None, :]).astype(
        jnp.int32
    )
    ranking = jnp.sum((jnp.cumsum(onehot, axis=0) - onehot) * onehot, axis=1)
    my_places = owners * capacity + ranking
    pair_local = jnp.arange(pairs_here, dtype=jnp.int32) // per_query
    entries = jnp.stack([pair_rows % passage_count, my_shard * query_count + pair_local], axis=1)
    table = (
        jnp.full((shard_total * capacity, 2), -1, jnp.int32)
        .at[my_places]
        .set(entries)
        .reshape(shard_total, capacity * 2)
    )

    y_total = lax.axis_size("y")
    rest_total = lax.axis_size("rest")
    my_y = lax.axis_index("y")
    along_y = [queries] + [
        lax.ppermute(queries, "y", [(i, (i + shift) % y_total) for i in range(y_total)])
        for shift in range(1, y_total)
    ]
    query_block = lax.all_gather(
        jnp.concatenate(along_y, axis=0), "rest", axis=0, tiled=True
    )
    mine = lax.all_to_all(table, shard, split_axis=0, concat_axis=0, tiled=True).reshape(
        shard_total, capacity, 2
    )

    flattened = query_block.reshape(-1, feature_width)
    scored = jnp.einsum("rd,cd->rc", flattened, centroids, preferred_element_type=jnp.float32)
    by_shift = jnp.max(scored, axis=1).reshape(rest_total, y_total, query_count, query_tokens)
    shift_of_y = (my_y - jnp.arange(y_total, dtype=jnp.int32)) % y_total
    local_best = (
        jnp.take(by_shift, shift_of_y, axis=1)
        .transpose(1, 0, 2, 3)
        .reshape(shard_total, query_count, query_tokens)
    )

    slot_table = jnp.maximum(mine[..., 0], 0).reshape(-1)
    global_query = jnp.maximum(mine[..., 1], 0).reshape(-1)
    source_shard = global_query // query_count
    query_table = (
        (source_shard % rest_total) * y_total + (my_y - source_shard // rest_total) % y_total
    ) * query_count + global_query % query_count
    asked = jnp.take(query_block, query_table, axis=0)
    chosen = jnp.take(passages, slot_table, axis=0)
    pair_scored = jnp.einsum("ntd,npd->ntp", asked, chosen, preferred_element_type=jnp.float32)
    token_index = lax.axis_index("cent") * token_rows + jnp.arange(token_rows, dtype=jnp.int32)
    valid_tokens = token_index[None, :] < jnp.take(lengths, slot_table, axis=0)[:, None]
    pair_scored = jnp.where(valid_tokens[:, None, :], pair_scored, masked_score)
    partial_value = jnp.max(pair_scored, axis=2)

    merged = jnp.concatenate([local_best.reshape(-1, query_tokens), partial_value], axis=0)
    cent_total = lax.axis_size("cent")
    arrived = [
        lax.ppermute(merged, "cent", [(i, (i + shift) % cent_total) for i in range(cent_total)])
        for shift in range(1, cent_total)
    ]
    for other in arrived:
        merged = jnp.maximum(merged, other)
    token_rows_out = shard_total * query_count
    best_all = merged[:token_rows_out].reshape(shard_total, query_count * query_tokens)
    complete = merged[token_rows_out:]
    pair_scores = (jnp.sum(complete, axis=1) / query_tokens).reshape(shard_total, capacity)

    outgoing = jnp.concatenate([best_all, pair_scores], axis=1)
    incoming = lax.all_to_all(outgoing, shard, split_axis=0, concat_axis=0, tiled=True)
    token_best = jnp.max(incoming[:, : query_count * query_tokens], axis=0).reshape(
        query_count, query_tokens
    )
    returned = incoming[:, query_count * query_tokens:]

    scores = jnp.take(returned.reshape(-1), my_places, axis=0).reshape(query_count, per_query)
    return (token_best, scores)


def solution(mesh):
    shard_size, cent_size = mesh.devices.shape
    y_size = len({d.coords[1] for d in mesh.devices.flat})
    split_mesh = Mesh(
        mesh.devices.reshape(y_size, shard_size // y_size, cent_size), ("y", "rest", "cent")
    )
    in_specs = (
        P(shard, None, None),
        P((*shard, "cent"), None),
        P(shard, "cent", None),
        P(shard),
        P(),
        P(shard, None),
    )
    out_specs = (P(shard, None), P(shard, None))
    return jax.shard_map(
        per_device, mesh=split_mesh, in_specs=in_specs, out_specs=out_specs, check_vma=False
    )
```

```python
import jax
import jax.numpy as jnp
from jax import lax
from jax.experimental import pallas as pl
from jax.sharding import Mesh, PartitionSpec as P

masked_score = -1e30


def centroid_best(rows, centroids):
    row_total, width = rows.shape
    block = 2048 if row_total % 2048 == 0 else row_total
    steps = row_total // block

    def kernel(row_ref, centroid_ref, out_ref):
        scored = lax.dot_general(
            centroid_ref[...], row_ref[...], (((1,), (1,)), ((), ())),
            preferred_element_type=jnp.float32,
        )
        out_ref[...] = jnp.max(scored, axis=0).reshape(1, 1, block)

    best = pl.pallas_call(
        kernel,
        grid=(steps,),
        in_specs=[
            pl.BlockSpec((block, width), lambda i: (i, 0)),
            pl.BlockSpec(centroids.shape, lambda i: (0, 0)),
        ],
        out_specs=pl.BlockSpec((1, 1, block), lambda i: (i, 0, 0)),
        out_shape=jax.ShapeDtypeStruct((steps, 1, block), jnp.float32),
    )(rows, centroids)
    return best.reshape(row_total)


shard = ("y", "rest")


def per_device(queries, centroids, passages, lengths, passage_row, candidates):
    query_count = queries.shape[0]
    query_tokens = queries.shape[1]
    feature_width = queries.shape[2]
    per_query = candidates.shape[1]
    passage_count = passages.shape[0]
    token_rows = passages.shape[1]
    shard_total = lax.axis_size(shard)
    capacity = max(2, 3 * query_count * per_query // shard_total)
    pairs_here = query_count * per_query
    my_shard = lax.axis_index(shard)

    pair_rows = jnp.take(passage_row, candidates.reshape(-1), axis=0)
    owners = pair_rows // passage_count
    onehot = (owners[:, None] == jnp.arange(shard_total, dtype=jnp.int32)[None, :]).astype(
        jnp.int32
    )
    ranking = jnp.sum((jnp.cumsum(onehot, axis=0) - onehot) * onehot, axis=1)
    my_places = owners * capacity + ranking
    pair_local = jnp.arange(pairs_here, dtype=jnp.int32) // per_query
    entries = jnp.stack([pair_rows % passage_count, my_shard * query_count + pair_local], axis=1)
    table = (
        jnp.full((shard_total * capacity, 2), -1, jnp.int32)
        .at[my_places]
        .set(entries)
        .reshape(shard_total, capacity * 2)
    )

    y_total = lax.axis_size("y")
    rest_total = lax.axis_size("rest")
    my_y = lax.axis_index("y")
    along_y = [queries] + [
        lax.ppermute(queries, "y", [(i, (i + shift) % y_total) for i in range(y_total)])
        for shift in range(1, y_total)
    ]
    query_block = lax.all_gather(
        jnp.concatenate(along_y, axis=0), "rest", axis=0, tiled=True
    )
    mine = lax.all_to_all(table, shard, split_axis=0, concat_axis=0, tiled=True).reshape(
        shard_total, capacity, 2
    )

    by_shift = centroid_best(query_block.reshape(-1, feature_width), centroids).reshape(
        rest_total, y_total, query_count, query_tokens
    )
    shift_of_y = (my_y - jnp.arange(y_total, dtype=jnp.int32)) % y_total
    local_best = (
        jnp.take(by_shift, shift_of_y, axis=1)
        .transpose(1, 0, 2, 3)
        .reshape(shard_total, query_count, query_tokens)
    )

    slot_table = jnp.maximum(mine[..., 0], 0).reshape(-1)
    global_query = jnp.maximum(mine[..., 1], 0).reshape(-1)
    source_shard = global_query // query_count
    query_table = (
        (source_shard % rest_total) * y_total + (my_y - source_shard // rest_total) % y_total
    ) * query_count + global_query % query_count
    asked = jnp.take(query_block, query_table, axis=0)
    chosen = jnp.take(passages, slot_table, axis=0)
    pair_scored = jnp.einsum("ntd,npd->ntp", asked, chosen, preferred_element_type=jnp.float32)
    token_index = lax.axis_index("cent") * token_rows + jnp.arange(token_rows, dtype=jnp.int32)
    valid_tokens = token_index[None, :] < jnp.take(lengths, slot_table, axis=0)[:, None]
    pair_scored = jnp.where(valid_tokens[:, None, :], pair_scored, masked_score)
    partial_value = jnp.max(pair_scored, axis=2)

    merged = jnp.concatenate([local_best.reshape(-1, query_tokens), partial_value], axis=0)
    cent_total = lax.axis_size("cent")
    arrived = [
        lax.ppermute(merged, "cent", [(i, (i + shift) % cent_total) for i in range(cent_total)])
        for shift in range(1, cent_total)
    ]
    for other in arrived:
        merged = jnp.maximum(merged, other)
    token_rows_out = shard_total * query_count
    best_all = merged[:token_rows_out].reshape(shard_total, query_count * query_tokens)
    complete = merged[token_rows_out:]
    pair_scores = (jnp.sum(complete, axis=1) / query_tokens).reshape(shard_total, capacity)

    outgoing = jnp.concatenate([best_all, pair_scores], axis=1)
    incoming = lax.all_to_all(outgoing, shard, split_axis=0, concat_axis=0, tiled=True)
    token_best = jnp.max(incoming[:, : query_count * query_tokens], axis=0).reshape(
        query_count, query_tokens
    )
    returned = incoming[:, query_count * query_tokens:]

    scores = jnp.take(returned.reshape(-1), my_places, axis=0).reshape(query_count, per_query)
    return (token_best, scores)


def solution(mesh):
    shard_size, cent_size = mesh.devices.shape
    y_size = len({d.coords[1] for d in mesh.devices.flat})
    split_mesh = Mesh(
        mesh.devices.reshape(y_size, shard_size // y_size, cent_size), ("y", "rest", "cent")
    )
    in_specs = (
        P(shard, None, None),
        P((*shard, "cent"), None),
        P(shard, "cent", None),
        P(shard),
        P(),
        P(shard, None),
    )
    out_specs = (P(shard, None), P(shard, None))
    return jax.shard_map(
        per_device, mesh=split_mesh, in_specs=in_specs, out_specs=out_specs, check_vma=False
    )
```

```python
import jax
import jax.numpy as jnp
from jax import lax
from jax.sharding import Mesh, PartitionSpec as P

masked_score = -1e30


shard = ("y", "rest")


def per_device(queries, centroids, passages, lengths, passage_row, candidates):
    query_count = queries.shape[0]
    query_tokens = queries.shape[1]
    feature_width = queries.shape[2]
    per_query = candidates.shape[1]
    passage_count = passages.shape[0]
    token_rows = passages.shape[1]
    shard_total = lax.axis_size(shard)
    capacity = max(2, 3 * query_count * per_query // shard_total)
    pairs_here = query_count * per_query
    my_shard = lax.axis_index(shard)

    pair_rows = jnp.take(passage_row, candidates.reshape(-1), axis=0)
    owners = pair_rows // passage_count
    onehot = (owners[:, None] == jnp.arange(shard_total, dtype=jnp.int32)[None, :]).astype(
        jnp.int32
    )
    ranking = jnp.sum((jnp.cumsum(onehot, axis=0) - onehot) * onehot, axis=1)
    my_places = owners * capacity + ranking
    pair_local = jnp.arange(pairs_here, dtype=jnp.int32) // per_query
    entries = jnp.stack([pair_rows % passage_count, my_shard * query_count + pair_local], axis=1)
    table = (
        jnp.full((shard_total * capacity, 2), -1, jnp.int32)
        .at[my_places]
        .set(entries)
        .reshape(shard_total, capacity * 2)
    )

    y_total = lax.axis_size("y")
    rest_total = lax.axis_size("rest")
    my_y = lax.axis_index("y")
    along_y = [queries] + [
        lax.ppermute(queries, "y", [(i, (i + shift) % y_total) for i in range(y_total)])
        for shift in range(1, y_total)
    ]
    query_block = lax.all_gather(
        jnp.concatenate(along_y, axis=0), "rest", axis=0, tiled=True
    )
    mine = lax.all_to_all(table, shard, split_axis=0, concat_axis=0, tiled=True).reshape(
        shard_total, capacity, 2
    )

    flattened = query_block.reshape(-1, feature_width)
    scored = jnp.einsum("rd,cd->rc", flattened, centroids, preferred_element_type=jnp.float32)
    by_shift = jnp.max(scored, axis=1).reshape(rest_total, y_total, query_count, query_tokens)
    shift_of_y = (my_y - jnp.arange(y_total, dtype=jnp.int32)) % y_total
    local_best = (
        jnp.take(by_shift, shift_of_y, axis=1)
        .transpose(1, 0, 2, 3)
        .reshape(shard_total, query_count, query_tokens)
    )

    slot_table = jnp.maximum(mine[..., 0], 0).reshape(-1)
    global_query = jnp.maximum(mine[..., 1], 0).reshape(-1)
    source_shard = global_query // query_count
    query_table = (
        (source_shard % rest_total) * y_total + (my_y - source_shard // rest_total) % y_total
    ) * query_count + global_query % query_count
    asked = jnp.take(query_block, query_table, axis=0)
    chosen = jnp.take(passages, slot_table, axis=0)
    pair_scored = jnp.einsum("ntd,npd->ntp", asked, chosen, preferred_element_type=jnp.float32)
    token_index = lax.axis_index("cent") * token_rows + jnp.arange(token_rows, dtype=jnp.int32)
    valid_tokens = token_index[None, :] < jnp.take(lengths, slot_table, axis=0)[:, None]
    pair_scored = jnp.where(valid_tokens[:, None, :], pair_scored, masked_score)
    partial_value = jnp.max(pair_scored, axis=2)

    cent_total = lax.axis_size("cent")

    def cent_max(values):
        arrived = [
            lax.ppermute(values, "cent", [(i, (i + shift) % cent_total) for i in range(cent_total)])
            for shift in range(1, cent_total)
        ]
        for other in arrived:
            values = jnp.maximum(values, other)
        return values

    complete = cent_max(partial_value)
    best_all = cent_max(local_best.reshape(shard_total, query_count * query_tokens))
    pair_scores = (jnp.sum(complete, axis=1) / query_tokens).reshape(shard_total, capacity)

    outgoing = jnp.concatenate([best_all, pair_scores], axis=1)
    incoming = lax.all_to_all(outgoing, shard, split_axis=0, concat_axis=0, tiled=True)
    token_best = jnp.max(incoming[:, : query_count * query_tokens], axis=0).reshape(
        query_count, query_tokens
    )
    returned = incoming[:, query_count * query_tokens:]

    scores = jnp.take(returned.reshape(-1), my_places, axis=0).reshape(query_count, per_query)
    return (token_best, scores)


def solution(mesh):
    shard_size, cent_size = mesh.devices.shape
    y_size = len({d.coords[1] for d in mesh.devices.flat})
    split_mesh = Mesh(
        mesh.devices.reshape(y_size, shard_size // y_size, cent_size), ("y", "rest", "cent")
    )
    in_specs = (
        P(shard, None, None),
        P((*shard, "cent"), None),
        P(shard, "cent", None),
        P(shard),
        P(),
        P(shard, None),
    )
    out_specs = (P(shard, None), P(shard, None))
    return jax.shard_map(
        per_device, mesh=split_mesh, in_specs=in_specs, out_specs=out_specs, check_vma=False
    )
```

```python
import jax
import jax.numpy as jnp
from jax import lax
from jax.sharding import Mesh, PartitionSpec as P

masked_score = -1e30


shard = ("y", "rest")


def per_device(queries, centroids, passages, lengths, passage_row, candidates):
    query_count = queries.shape[0]
    query_tokens = queries.shape[1]
    feature_width = queries.shape[2]
    per_query = candidates.shape[1]
    passage_count = passages.shape[0]
    token_rows = passages.shape[1]
    shard_total = lax.axis_size(shard)
    capacity = max(2, 3 * query_count * per_query // shard_total)
    pairs_here = query_count * per_query
    my_shard = lax.axis_index(shard)

    pair_rows = jnp.take(passage_row, candidates.reshape(-1), axis=0)
    owners = pair_rows // passage_count
    onehot = (owners[:, None] == jnp.arange(shard_total, dtype=jnp.int32)[None, :]).astype(
        jnp.int32
    )
    ranking = jnp.sum((jnp.cumsum(onehot, axis=0) - onehot) * onehot, axis=1)
    my_places = owners * capacity + ranking
    pair_local = jnp.arange(pairs_here, dtype=jnp.int32) // per_query
    entries = jnp.stack([pair_rows % passage_count, my_shard * query_count + pair_local], axis=1)
    table = (
        jnp.full((shard_total * capacity, 2), -1, jnp.int32)
        .at[my_places]
        .set(entries)
        .reshape(shard_total, capacity * 2)
    )

    y_total = lax.axis_size("y")
    rest_total = lax.axis_size("rest")
    my_y = lax.axis_index("y")
    along_y = [queries] + [
        lax.ppermute(queries, "y", [(i, (i + shift) % y_total) for i in range(y_total)])
        for shift in range(1, y_total)
    ]
    query_block = lax.all_gather(
        jnp.concatenate(along_y, axis=0), "rest", axis=0, tiled=True
    )
    mine = lax.all_to_all(table, shard, split_axis=0, concat_axis=0, tiled=True).reshape(
        shard_total, capacity, 2
    )

    cent_total = lax.axis_size("cent")

    def cent_max(values):
        arrived = [
            lax.ppermute(values, "cent", [(i, (i + shift) % cent_total) for i in range(cent_total)])
            for shift in range(1, cent_total)
        ]
        for other in arrived:
            values = jnp.maximum(values, other)
        return values

    shift_of_y = (my_y - jnp.arange(y_total, dtype=jnp.int32)) % y_total
    halves = 2 if rest_total % 2 == 0 else 1
    rest_part = rest_total // halves
    rows_per = rest_part * y_total * query_count
    best_parts = []
    for half in range(halves):
        block = query_block[half * rows_per:(half + 1) * rows_per].reshape(-1, feature_width)
        scored = jnp.einsum("rd,cd->rc", block, centroids, preferred_element_type=jnp.float32)
        by_shift = jnp.max(scored, axis=1).reshape(rest_part, y_total, query_count * query_tokens)
        best_parts.append(cent_max(jnp.take(by_shift, shift_of_y, axis=1).transpose(1, 0, 2)))

    slot_table = jnp.maximum(mine[..., 0], 0).reshape(-1)
    global_query = jnp.maximum(mine[..., 1], 0).reshape(-1)
    source_shard = global_query // query_count
    query_table = (
        (source_shard % rest_total) * y_total + (my_y - source_shard // rest_total) % y_total
    ) * query_count + global_query % query_count
    asked = jnp.take(query_block, query_table, axis=0)
    chosen = jnp.take(passages, slot_table, axis=0)
    pair_scored = jnp.einsum("ntd,npd->ntp", asked, chosen, preferred_element_type=jnp.float32)
    token_index = lax.axis_index("cent") * token_rows + jnp.arange(token_rows, dtype=jnp.int32)
    valid_tokens = token_index[None, :] < jnp.take(lengths, slot_table, axis=0)[:, None]
    pair_scored = jnp.where(valid_tokens[:, None, :], pair_scored, masked_score)
    partial_value = jnp.max(pair_scored, axis=2)

    complete = cent_max(partial_value)
    best_all = jnp.concatenate(best_parts, axis=1).reshape(shard_total, query_count * query_tokens)
    pair_scores = (jnp.sum(complete, axis=1) / query_tokens).reshape(shard_total, capacity)

    outgoing = jnp.concatenate([best_all, pair_scores], axis=1)
    incoming = lax.all_to_all(outgoing, shard, split_axis=0, concat_axis=0, tiled=True)
    token_best = jnp.max(incoming[:, : query_count * query_tokens], axis=0).reshape(
        query_count, query_tokens
    )
    returned = incoming[:, query_count * query_tokens:]

    scores = jnp.take(returned.reshape(-1), my_places, axis=0).reshape(query_count, per_query)
    return (token_best, scores)


def solution(mesh):
    shard_size, cent_size = mesh.devices.shape
    y_size = len({d.coords[1] for d in mesh.devices.flat})
    split_mesh = Mesh(
        mesh.devices.reshape(y_size, shard_size // y_size, cent_size), ("y", "rest", "cent")
    )
    in_specs = (
        P(shard, None, None),
        P((*shard, "cent"), None),
        P(shard, "cent", None),
        P(shard),
        P(),
        P(shard, None),
    )
    out_specs = (P(shard, None), P(shard, None))
    return jax.shard_map(
        per_device, mesh=split_mesh, in_specs=in_specs, out_specs=out_specs, check_vma=False
    )
```

```python
import jax
import jax.numpy as jnp
from jax import lax
from jax.sharding import Mesh, PartitionSpec as P

masked_score = -1e30


shard = ("y", "rest")


def per_device(queries, centroids, passages, lengths, passage_row, candidates):
    query_count = queries.shape[0]
    query_tokens = queries.shape[1]
    feature_width = queries.shape[2]
    per_query = candidates.shape[1]
    passage_count = passages.shape[0]
    token_rows = passages.shape[1]
    shard_total = lax.axis_size(shard)
    capacity = max(2, 3 * query_count * per_query // shard_total)
    pairs_here = query_count * per_query
    my_shard = lax.axis_index(shard)

    pair_rows = jnp.take(passage_row, candidates.reshape(-1), axis=0)
    owners = pair_rows // passage_count
    onehot = (owners[:, None] == jnp.arange(shard_total, dtype=jnp.int32)[None, :]).astype(
        jnp.int32
    )
    ranking = jnp.sum((jnp.cumsum(onehot, axis=0) - onehot) * onehot, axis=1)
    my_places = owners * capacity + ranking
    pair_local = jnp.arange(pairs_here, dtype=jnp.int32) // per_query
    entries = jnp.stack([pair_rows % passage_count, my_shard * query_count + pair_local], axis=1)
    table = (
        jnp.full((shard_total * capacity, 2), -1, jnp.int32)
        .at[my_places]
        .set(entries)
        .reshape(shard_total, capacity * 2)
    )

    y_total = lax.axis_size("y")
    rest_total = lax.axis_size("rest")
    my_y = lax.axis_index("y")
    along_y = [queries] + [
        lax.ppermute(queries, "y", [(i, (i + shift) % y_total) for i in range(y_total)])
        for shift in range(1, y_total)
    ]
    query_block = lax.all_gather(
        jnp.concatenate(along_y, axis=0), "rest", axis=0, tiled=True
    )
    mine = lax.all_to_all(table, shard, split_axis=0, concat_axis=0, tiled=True).reshape(
        shard_total, capacity, 2
    )

    flattened = query_block.reshape(-1, feature_width)
    scored = jnp.einsum("rd,cd->rc", flattened, centroids, preferred_element_type=jnp.float32)
    by_shift = jnp.max(scored, axis=1).reshape(rest_total, y_total, query_count, query_tokens)
    shift_of_y = (my_y - jnp.arange(y_total, dtype=jnp.int32)) % y_total
    local_best = (
        jnp.take(by_shift, shift_of_y, axis=1)
        .transpose(1, 0, 2, 3)
        .reshape(shard_total, query_count, query_tokens)
    )

    slot_table = jnp.maximum(mine[..., 0], 0).reshape(-1)
    global_query = jnp.maximum(mine[..., 1], 0).reshape(-1)
    source_shard = global_query // query_count
    query_table = (
        (source_shard % rest_total) * y_total + (my_y - source_shard // rest_total) % y_total
    ) * query_count + global_query % query_count
    asked = jnp.take(query_block, query_table, axis=0)
    chosen = jnp.take(passages, slot_table, axis=0)
    pair_scored = jnp.einsum("ntd,npd->ntp", asked, chosen, preferred_element_type=jnp.float32)
    token_index = lax.axis_index("cent") * token_rows + jnp.arange(token_rows, dtype=jnp.int32)
    valid_tokens = token_index[None, :] < jnp.take(lengths, slot_table, axis=0)[:, None]
    pair_scored = jnp.where(valid_tokens[:, None, :], pair_scored, masked_score)
    partial_value = jnp.max(pair_scored, axis=2)

    cent_total = lax.axis_size("cent")

    def cent_max(values):
        arrived = [
            lax.ppermute(values, "cent", [(i, (i + shift) % cent_total) for i in range(cent_total)])
            for shift in range(1, cent_total)
        ]
        for other in arrived:
            values = jnp.maximum(values, other)
        return values

    complete = cent_max(partial_value)
    best_all = local_best.reshape(shard_total, query_count * query_tokens)
    pair_scores = (jnp.sum(complete, axis=1) / query_tokens).reshape(shard_total, capacity)

    outgoing = jnp.concatenate([best_all, pair_scores], axis=1)
    incoming = lax.all_to_all(outgoing, shard, split_axis=0, concat_axis=0, tiled=True)
    token_best = cent_max(
        jnp.max(incoming[:, : query_count * query_tokens], axis=0).reshape(
            query_count, query_tokens
        )
    )
    returned = incoming[:, query_count * query_tokens:]

    scores = jnp.take(returned.reshape(-1), my_places, axis=0).reshape(query_count, per_query)
    return (token_best, scores)


def solution(mesh):
    shard_size, cent_size = mesh.devices.shape
    y_size = len({d.coords[1] for d in mesh.devices.flat})
    split_mesh = Mesh(
        mesh.devices.reshape(y_size, shard_size // y_size, cent_size), ("y", "rest", "cent")
    )
    in_specs = (
        P(shard, None, None),
        P((*shard, "cent"), None),
        P(shard, "cent", None),
        P(shard),
        P(),
        P(shard, None),
    )
    out_specs = (P(shard, None), P(shard, None))
    return jax.shard_map(
        per_device, mesh=split_mesh, in_specs=in_specs, out_specs=out_specs, check_vma=False
    )
```

```python
import jax
import jax.numpy as jnp
from jax import lax
from jax.sharding import Mesh, PartitionSpec as P

masked_score = -1e30


shard = ("y", "rest")


def per_device(queries, centroids, passages, lengths, passage_row, candidates):
    query_count = queries.shape[0]
    query_tokens = queries.shape[1]
    feature_width = queries.shape[2]
    per_query = candidates.shape[1]
    passage_count = passages.shape[0]
    token_rows = passages.shape[1]
    shard_total = lax.axis_size(shard)
    capacity = max(2, 3 * query_count * per_query // shard_total)
    pairs_here = query_count * per_query
    my_shard = lax.axis_index(shard)

    pair_rows = jnp.take(passage_row, candidates.reshape(-1), axis=0)
    owners = pair_rows // passage_count
    onehot = (owners[:, None] == jnp.arange(shard_total, dtype=jnp.int32)[None, :]).astype(
        jnp.int32
    )
    ranking = jnp.sum((jnp.cumsum(onehot, axis=0) - onehot) * onehot, axis=1)
    my_places = owners * capacity + ranking
    pair_local = jnp.arange(pairs_here, dtype=jnp.int32) // per_query
    entries = jnp.stack([pair_rows % passage_count, my_shard * query_count + pair_local], axis=1)
    table = (
        jnp.full((shard_total * capacity, 2), -1, jnp.int32)
        .at[my_places]
        .set(entries)
        .reshape(shard_total, capacity * 2)
    )

    y_total = lax.axis_size("y")
    rest_total = lax.axis_size("rest")
    my_y = lax.axis_index("y")
    along_y = [queries] + [
        lax.ppermute(queries, "y", [(i, (i + shift) % y_total) for i in range(y_total)])
        for shift in range(1, y_total)
    ]
    query_block = lax.all_gather(
        jnp.concatenate(along_y, axis=0), "rest", axis=0, tiled=True
    )
    mine = lax.all_to_all(table, shard, split_axis=0, concat_axis=0, tiled=True).reshape(
        shard_total, capacity, 2
    )

    flattened = query_block.reshape(-1, feature_width)
    scored = jnp.einsum("rd,cd->rc", flattened, centroids, preferred_element_type=jnp.float32)
    by_shift = jnp.max(scored, axis=1).reshape(rest_total, y_total, query_count, query_tokens)
    shift_of_y = (my_y - jnp.arange(y_total, dtype=jnp.int32)) % y_total
    local_best = (
        jnp.take(by_shift, shift_of_y, axis=1)
        .transpose(1, 0, 2, 3)
        .reshape(shard_total, query_count, query_tokens)
    )

    slot_table = jnp.maximum(mine[..., 0], 0).reshape(-1)
    global_query = jnp.maximum(mine[..., 1], 0).reshape(-1)
    source_shard = global_query // query_count
    query_table = (
        (source_shard % rest_total) * y_total + (my_y - source_shard // rest_total) % y_total
    ) * query_count + global_query % query_count
    token_index = lax.axis_index("cent") * token_rows + jnp.arange(token_rows, dtype=jnp.int32)

    def pair_maxima(query_rows, slot_rows):
        asked = jnp.take(query_block, query_rows, axis=0)
        chosen = jnp.take(passages, slot_rows, axis=0)
        pair_scored = jnp.einsum("ntd,npd->ntp", asked, chosen, preferred_element_type=jnp.float32)
        valid_tokens = token_index[None, :] < jnp.take(lengths, slot_rows, axis=0)[:, None]
        pair_scored = jnp.where(valid_tokens[:, None, :], pair_scored, masked_score)
        return jnp.max(pair_scored, axis=2)

    cent_total = lax.axis_size("cent")

    def cent_max(values):
        arrived = [
            lax.ppermute(values, "cent", [(i, (i + shift) % cent_total) for i in range(cent_total)])
            for shift in range(1, cent_total)
        ]
        for other in arrived:
            values = jnp.maximum(values, other)
        return values

    pair_total = shard_total * capacity
    pair_halves = 2 if pair_total % 2 == 0 else 1
    half_size = pair_total // pair_halves
    complete = jnp.concatenate(
        [
            cent_max(
                pair_maxima(
                    query_table[h * half_size:(h + 1) * half_size],
                    slot_table[h * half_size:(h + 1) * half_size],
                )
            )
            for h in range(pair_halves)
        ],
        axis=0,
    )
    best_all = local_best.reshape(shard_total, query_count * query_tokens)
    pair_scores = (jnp.sum(complete, axis=1) / query_tokens).reshape(shard_total, capacity)

    outgoing = jnp.concatenate([best_all, pair_scores], axis=1)
    incoming = lax.all_to_all(outgoing, shard, split_axis=0, concat_axis=0, tiled=True)
    token_best = cent_max(
        jnp.max(incoming[:, : query_count * query_tokens], axis=0).reshape(
            query_count, query_tokens
        )
    )
    returned = incoming[:, query_count * query_tokens:]

    scores = jnp.take(returned.reshape(-1), my_places, axis=0).reshape(query_count, per_query)
    return (token_best, scores)


def solution(mesh):
    shard_size, cent_size = mesh.devices.shape
    y_size = len({d.coords[1] for d in mesh.devices.flat})
    split_mesh = Mesh(
        mesh.devices.reshape(y_size, shard_size // y_size, cent_size), ("y", "rest", "cent")
    )
    in_specs = (
        P(shard, None, None),
        P((*shard, "cent"), None),
        P(shard, "cent", None),
        P(shard),
        P(),
        P(shard, None),
    )
    out_specs = (P(shard, None), P(shard, None))
    return jax.shard_map(
        per_device, mesh=split_mesh, in_specs=in_specs, out_specs=out_specs, check_vma=False
    )
```

```python
import jax
import jax.numpy as jnp
from jax import lax
from jax.sharding import Mesh, PartitionSpec as P

masked_score = -1e30


shard = ("y", "rest")


def per_device(queries, centroids, passages, lengths, passage_row, candidates):
    query_count = queries.shape[0]
    query_tokens = queries.shape[1]
    feature_width = queries.shape[2]
    per_query = candidates.shape[1]
    passage_count = passages.shape[0]
    token_rows = passages.shape[1]
    shard_total = lax.axis_size(shard)
    capacity = max(2, 3 * query_count * per_query // shard_total)
    pairs_here = query_count * per_query
    my_shard = lax.axis_index(shard)

    pair_rows = jnp.take(passage_row, candidates.reshape(-1), axis=0)
    owners = pair_rows // passage_count
    onehot = (owners[:, None] == jnp.arange(shard_total, dtype=jnp.int32)[None, :]).astype(
        jnp.int32
    )
    ranking = jnp.sum((jnp.cumsum(onehot, axis=0) - onehot) * onehot, axis=1)
    my_places = owners * capacity + ranking
    pair_local = jnp.arange(pairs_here, dtype=jnp.int32) // per_query
    entries = jnp.stack([pair_rows % passage_count, my_shard * query_count + pair_local], axis=1)
    table = (
        jnp.full((shard_total * capacity, 2), -1, jnp.int32)
        .at[my_places]
        .set(entries)
        .reshape(shard_total, capacity * 2)
    )

    y_total = lax.axis_size("y")
    rest_total = lax.axis_size("rest")
    my_y = lax.axis_index("y")
    along_y = [queries] + [
        lax.ppermute(queries, "y", [(i, (i + shift) % y_total) for i in range(y_total)])
        for shift in range(1, y_total)
    ]
    query_block = lax.all_gather(
        jnp.concatenate(along_y, axis=0), "rest", axis=0, tiled=True
    )
    mine = lax.all_to_all(table, shard, split_axis=0, concat_axis=0, tiled=True).reshape(
        shard_total, capacity, 2
    )

    flattened = query_block.reshape(-1, feature_width)
    scored = jnp.einsum("rd,cd->rc", flattened, centroids, preferred_element_type=jnp.float32)
    by_shift = jnp.max(scored, axis=1).reshape(rest_total, y_total, query_count, query_tokens)
    shift_of_y = (my_y - jnp.arange(y_total, dtype=jnp.int32)) % y_total
    local_best = (
        jnp.take(by_shift, shift_of_y, axis=1)
        .transpose(1, 0, 2, 3)
        .reshape(shard_total, query_count, query_tokens)
    )

    slot_table = jnp.maximum(mine[..., 0], 0).reshape(-1)
    global_query = jnp.maximum(mine[..., 1], 0).reshape(-1)
    source_shard = global_query // query_count
    query_table = (
        (source_shard % rest_total) * y_total + (my_y - source_shard // rest_total) % y_total
    ) * query_count + global_query % query_count
    asked = jnp.take(query_block, query_table, axis=0)
    chosen = jnp.take(passages, slot_table, axis=0)
    pair_scored = jnp.einsum("ntd,npd->ntp", asked, chosen, preferred_element_type=jnp.float32)
    token_index = lax.axis_index("cent") * token_rows + jnp.arange(token_rows, dtype=jnp.int32)
    valid_tokens = token_index[None, :] < jnp.take(lengths, slot_table, axis=0)[:, None]
    pair_scored = jnp.where(valid_tokens[:, None, :], pair_scored, masked_score)
    partial_value = jnp.max(pair_scored, axis=2)

    cent_total = lax.axis_size("cent")

    def cent_max(values):
        arrived = [
            lax.ppermute(values, "cent", [(i, (i + shift) % cent_total) for i in range(cent_total)])
            for shift in range(1, cent_total)
        ]
        for other in arrived:
            values = jnp.maximum(values, other)
        return values

    best_all = local_best.reshape(shard_total, query_count * query_tokens)
    pair_partials = partial_value.reshape(shard_total, capacity * query_tokens)

    outgoing = jnp.concatenate([best_all, pair_partials], axis=1)
    incoming = lax.all_to_all(outgoing, shard, split_axis=0, concat_axis=0, tiled=True)
    token_part = jnp.max(incoming[:, : query_count * query_tokens], axis=0).reshape(
        query_count, query_tokens
    )
    pair_part = jnp.take(
        incoming[:, query_count * query_tokens:].reshape(-1, query_tokens), my_places, axis=0
    )
    merged = cent_max(jnp.concatenate([token_part, pair_part], axis=0))
    token_best = merged[:query_count]
    scores = (jnp.sum(merged[query_count:], axis=1) / query_tokens).reshape(query_count, per_query)
    return (token_best, scores)


def solution(mesh):
    shard_size, cent_size = mesh.devices.shape
    y_size = len({d.coords[1] for d in mesh.devices.flat})
    split_mesh = Mesh(
        mesh.devices.reshape(y_size, shard_size // y_size, cent_size), ("y", "rest", "cent")
    )
    in_specs = (
        P(shard, None, None),
        P((*shard, "cent"), None),
        P(shard, "cent", None),
        P(shard),
        P(),
        P(shard, None),
    )
    out_specs = (P(shard, None), P(shard, None))
    return jax.shard_map(
        per_device, mesh=split_mesh, in_specs=in_specs, out_specs=out_specs, check_vma=False
    )
```

```python
import jax
import jax.numpy as jnp
from jax import lax
from jax.sharding import Mesh, PartitionSpec as P

masked_score = -1e30


shard = ("y", "rest")


def per_device(queries, centroids, passages, lengths, passage_row, candidates):
    query_count = queries.shape[0]
    query_tokens = queries.shape[1]
    feature_width = queries.shape[2]
    per_query = candidates.shape[1]
    passage_count = passages.shape[0]
    token_rows = passages.shape[1]
    shard_total = lax.axis_size(shard)
    capacity = max(2, 3 * query_count * per_query // shard_total)
    pairs_here = query_count * per_query
    my_shard = lax.axis_index(shard)

    pair_rows = jnp.take(passage_row, candidates.reshape(-1), axis=0)
    owners = pair_rows // passage_count
    onehot = (owners[:, None] == jnp.arange(shard_total, dtype=jnp.int32)[None, :]).astype(
        jnp.int32
    )
    ranking = jnp.sum((jnp.cumsum(onehot, axis=0) - onehot) * onehot, axis=1)
    my_places = owners * capacity + ranking
    pair_local = jnp.arange(pairs_here, dtype=jnp.int32) // per_query
    entries = jnp.stack([pair_rows % passage_count, my_shard * query_count + pair_local], axis=1)
    table = (
        jnp.full((shard_total * capacity, 2), -1, jnp.int32)
        .at[my_places]
        .set(entries)
        .reshape(shard_total, capacity * 2)
    )

    y_total = lax.axis_size("y")
    rest_total = lax.axis_size("rest")
    my_y = lax.axis_index("y")
    along_y = [queries] + [
        lax.ppermute(queries, "y", [(i, (i + shift) % y_total) for i in range(y_total)])
        for shift in range(1, y_total)
    ]
    query_block = lax.all_gather(
        jnp.concatenate(along_y, axis=0), "rest", axis=0, tiled=True
    )
    mine = lax.all_to_all(table, shard, split_axis=0, concat_axis=0, tiled=True).reshape(
        shard_total, capacity, 2
    )

    slot_table = jnp.maximum(mine[..., 0], 0).reshape(-1)
    global_query = jnp.maximum(mine[..., 1], 0).reshape(-1)
    source_shard = global_query // query_count
    query_table = (
        (source_shard % rest_total) * y_total + (my_y - source_shard // rest_total) % y_total
    ) * query_count + global_query % query_count
    asked = jnp.take(query_block, query_table, axis=0)
    chosen = jnp.take(passages, slot_table, axis=0)
    pair_scored = jnp.einsum("ntd,npd->ntp", asked, chosen, preferred_element_type=jnp.float32)
    token_index = lax.axis_index("cent") * token_rows + jnp.arange(token_rows, dtype=jnp.int32)
    valid_tokens = token_index[None, :] < jnp.take(lengths, slot_table, axis=0)[:, None]
    pair_scored = jnp.where(valid_tokens[:, None, :], pair_scored, masked_score)
    partial_value = jnp.max(pair_scored, axis=2)

    ordered_block, partial_value = lax.optimization_barrier((query_block, partial_value))
    flattened = ordered_block.reshape(-1, feature_width)
    scored = jnp.einsum("rd,cd->rc", flattened, centroids, preferred_element_type=jnp.float32)
    by_shift = jnp.max(scored, axis=1).reshape(rest_total, y_total, query_count, query_tokens)
    shift_of_y = (my_y - jnp.arange(y_total, dtype=jnp.int32)) % y_total
    local_best = (
        jnp.take(by_shift, shift_of_y, axis=1)
        .transpose(1, 0, 2, 3)
        .reshape(shard_total, query_count, query_tokens)
    )

    cent_total = lax.axis_size("cent")

    def cent_max(values):
        arrived = [
            lax.ppermute(values, "cent", [(i, (i + shift) % cent_total) for i in range(cent_total)])
            for shift in range(1, cent_total)
        ]
        for other in arrived:
            values = jnp.maximum(values, other)
        return values

    best_all = local_best.reshape(shard_total, query_count * query_tokens)
    pair_partials = partial_value.reshape(shard_total, capacity * query_tokens)

    outgoing = jnp.concatenate([best_all, pair_partials], axis=1)
    incoming = lax.all_to_all(outgoing, shard, split_axis=0, concat_axis=0, tiled=True)
    token_part = jnp.max(incoming[:, : query_count * query_tokens], axis=0).reshape(
        query_count, query_tokens
    )
    pair_part = jnp.take(
        incoming[:, query_count * query_tokens:].reshape(-1, query_tokens), my_places, axis=0
    )
    merged = cent_max(jnp.concatenate([token_part, pair_part], axis=0))
    token_best = merged[:query_count]
    scores = (jnp.sum(merged[query_count:], axis=1) / query_tokens).reshape(query_count, per_query)
    return (token_best, scores)


def solution(mesh):
    shard_size, cent_size = mesh.devices.shape
    y_size = len({d.coords[1] for d in mesh.devices.flat})
    split_mesh = Mesh(
        mesh.devices.reshape(y_size, shard_size // y_size, cent_size), ("y", "rest", "cent")
    )
    in_specs = (
        P(shard, None, None),
        P((*shard, "cent"), None),
        P(shard, "cent", None),
        P(shard),
        P(),
        P(shard, None),
    )
    out_specs = (P(shard, None), P(shard, None))
    return jax.shard_map(
        per_device, mesh=split_mesh, in_specs=in_specs, out_specs=out_specs, check_vma=False
    )
```
